256 devices in a mesh: dp: 32 (over z, x), seq: 8 (over y, core).
Axes of the slice: x: 4, y: 4, z: 8, core: 2. Of those that a mesh axis runs over, the one named last changes fastest.
Arguments:
- hidden: bfloat16 [32, 2048, 4096], P('dp', 'seq'), may hold values from -6 to 6
- base_query_weight: bfloat16 [32, 2048, 4096], P('dp', 'seq'), may hold values from -120 to 120
- base_key_weight: bfloat16 [32, 2048, 1024], P('dp', 'seq'), may hold values from -6 to 6
- base_value_weight: bfloat16 [32, 2048, 1024], P('dp', 'seq'), may hold values from -6 to 6
- lengths: int32 [32, 16], P('dp'), may hold values from 1 to 512, 2048 in all within a row
- request_adapter: int32 [32, 16], replicated, may hold values from 0 to 255, as said below
- adapter_pool_row: int32 [256], replicated, may hold values from 0 to 255, as said below
- adapter_down_weight: bfloat16 [256, 4096, 256], P('dp', 'seq'), may hold values from -0.09375 to 0.09375
- adapter_up_query: bfloat16 [256, 64, 4096], P('dp', None, 'seq'), may hold values from -0.23925781 to 0.23925781
- adapter_up_key_value: bfloat16 [256, 2, 64, 1024], P('dp', None, None, 'seq'), may hold values from -0.23925781 to 0.23925781
- adapter_up_output: bfloat16 [256, 64, 4096], P('dp', None, 'seq'), may hold values from -0.71875 to 0.71875
Outputs:
- context: bfloat16 [32, 2048, 4096], P('dp', 'seq')
- adapter_out: bfloat16 [32, 2048, 4096], P('dp', 'seq')
The draws below stay inside these ranges and needn't reach their ends.
Inputs may be any that keep to these rules, and one draw needn't show every extreme that they name: `request_adapter`: within a group the 16 adapters differ. At most 1 of one group's adapters have pool rows (adapter_pool_row) held by one index of dp, that index being the pool row divided by 8, and in every group some index of dp holds exactly 1 of them. `adapter_pool_row`: every pool row is named by exactly one adapter.
All inputs are finite; a program needn't handle non-finite values.
Results may differ from the reference program's by a relative error of at most 0.017.
Values may be sent and summed in bfloat16 or wider, within the bound.
No kernel may reach another device: no remote copies, remote signals or barrier semaphores. Data moves between devices by JAX's collectives and lax.ppermute only.
A program may use at most 128 MiB of HBM per device.

```python
import math
import jax
import jax.numpy as jnp
import numpy as np
from jax import lax

QUERY_HEADS = 32
KEY_VALUE_HEADS = 8
HEAD_SIZE = 128
MODEL_WIDTH = 4096
ADAPTER_RANK = 64
REQS = 16
ADP_DEV = 8
GROUP_TOKENS = 2048
LONGEST_REQUEST = 512
REQUEST_GROUPS = 32
ADAPTER_POOL = 256
CAP = 1


def paired_heads(key):
    random_key_split = jax.random.fold_in(key, 7)
    key_queries = jax.random.fold_in(key, 8)
    sampled_keys = jnp.clip(jax.random.normal(random_key_split, (REQUEST_GROUPS, GROUP_TOKENS, KEY_VALUE_HEADS * HEAD_SIZE), jnp.float32), -6.0, 6.0)
    query_rows = jnp.clip(jax.random.normal(key_queries, (REQUEST_GROUPS, GROUP_TOKENS, QUERY_HEADS * HEAD_SIZE), jnp.float32), -6.0, 6.0)
    return (query_rows, sampled_keys)


def draw_base_query_weight(key, part):
    return paired_heads(key)[0].astype(jnp.bfloat16)


def draw_base_key_weight(key, part):
    return paired_heads(key)[1].astype(jnp.bfloat16)


def routing(key):
    row_order = jax.random.permutation(jax.random.fold_in(key, 21), ADAPTER_POOL).astype(jnp.int32)
    inverse = jnp.zeros((ADAPTER_POOL,), jnp.int32).at[row_order].set(jnp.arange(ADAPTER_POOL, dtype=jnp.int32))
    entries = REQUEST_GROUPS * CAP
    holder = jnp.arange(entries, dtype=jnp.int32) // CAP
    copies = jnp.arange(entries, dtype=jnp.int32) % CAP

    def one_group(group_key_rows):
        key_forced, key_score, key_shuffle, key_shift = jax.random.split(group_key_rows, 4)
        forced = jax.random.randint(key_forced, (), 0, REQUEST_GROUPS)
        scores = jax.random.permutation(key_score, entries).astype(jnp.int32) + 1
        scores = jnp.where(holder == forced, 0, scores)
        chosen = jnp.argsort(scores, stable=True)[:REQS]
        chosen = chosen[jax.random.permutation(key_shuffle, REQS)]
        shifts = jax.random.randint(key_shift, (REQUEST_GROUPS,), 0, ADP_DEV)
        holders = holder[chosen]
        places = holders * ADP_DEV + (copies[chosen] + shifts[holders]) % ADP_DEV
        return inverse[places]
    request_table = jax.vmap(one_group)(jax.random.split(jax.random.fold_in(key, 22), REQUEST_GROUPS))
    return (row_order, request_table.astype(jnp.int32))


def draw_request_adapter(key, part):
    return routing(key)[1]


def draw_adapter_pool_row(key, part):
    return routing(key)[0]


def level_of(own_key, dims, shards, low, top_value):
    factor_of, own = 1.0, jax.random.fold_in(own_key, 6)
    for axis_at, shards_of in shards:
        heights = jnp.exp(jax.random.uniform(jax.random.fold_in(own, axis_at), (shards_of,), jnp.float32, low / len(shards), top_value / len(shards)))
        factor_of = factor_of * jnp.repeat(heights, dims[axis_at] // shards_of).reshape([-1 if axis == axis_at else 1 for axis in range(len(dims))])
    return factor_of


def split_up(number_of, total, limit, skew):
    weights = [(1 << 20) // math.isqrt(standing ** skew) + 1 for standing in range(2, number_of + 1)]
    rest, counts = total - limit - (number_of - 1), [1] * (number_of - 1)
    while rest > 0:
        movable = [i for i in range(number_of - 1) if counts[i] < limit]
        pool, left = sum([weights[i] for i in movable]), rest
        for i in movable:
            extra = min(limit - counts[i], max(1, left * weights[i] // pool), rest)
            counts[i] = counts[i] + extra
            rest = rest - extra
    return np.array([limit] + counts)


def ragged(stream_key, count, total, limit, lean):
    if count == 2:
        one = jax.random.randint(stream_key, (), max(1, total - limit), min(limit, total - 1) + 1)
        return jnp.stack([one, total - one])
    sizes = jnp.asarray(split_up(count, total, limit, lean), jnp.int32)
    pairs = (count - 1) // 2
    giver, taker = sizes[1:1 + 2 * pairs:2], sizes[2:2 + 2 * pairs:2]
    slack = jnp.minimum(giver - 1, limit - taker)
    passed = jax.random.randint(jax.random.fold_in(stream_key, 1), (pairs,), 0, 1 << 20) % (slack + 1)
    sizes = sizes.at[1:1 + 2 * pairs:2].set(giver - passed).at[2:2 + 2 * pairs:2].set(taker + passed)
    return sizes[jax.random.permutation(jax.random.fold_in(stream_key, 2), count)]


def normal_values(key, extent, deviation, bound, pieces=(), kind=jnp.bfloat16):
    values = deviation * jax.random.normal(key, extent, jnp.float32)
    if pieces:
        values = values * level_of(key, extent, pieces, -0.22, 0.18)
    return jnp.clip(values, -bound, bound).astype(kind)


def setup_inputs(seed: int = 0) -> dict:
    streams_of = jax.random.split(jax.random.key(seed), 12)
    return {
        "hidden": normal_values(streams_of[0], (REQUEST_GROUPS, GROUP_TOKENS, MODEL_WIDTH), 1.0, 6.0, ((0, 32), (1, 8))),
        "base_query_weight": draw_base_query_weight(jax.random.fold_in(streams_of[11], 71), 0),
        "base_key_weight": draw_base_key_weight(jax.random.fold_in(streams_of[11], 71), 0),
        "base_value_weight": normal_values(streams_of[3], (REQUEST_GROUPS, GROUP_TOKENS, KEY_VALUE_HEADS * HEAD_SIZE), 1.0, 6.0, ((0, 32), (1, 8))),
        "lengths": jax.vmap(lambda own: ragged(own, REQS, GROUP_TOKENS, LONGEST_REQUEST, 2))(jax.random.split(streams_of[4], REQUEST_GROUPS)).reshape((REQUEST_GROUPS, REQS)).astype(jnp.int32),
        "request_adapter": draw_request_adapter(jax.random.fold_in(streams_of[11], 71), 0),
        "adapter_pool_row": draw_adapter_pool_row(jax.random.fold_in(streams_of[11], 71), 0),
        "adapter_down_weight": normal_values(streams_of[7], (ADAPTER_POOL, MODEL_WIDTH, 4 * ADAPTER_RANK), MODEL_WIDTH ** -0.5, 0.09375, ((0, 32), (1, 8))),
        "adapter_up_query": normal_values(streams_of[8], (ADAPTER_POOL, ADAPTER_RANK, MODEL_WIDTH), 0.04, 0.23925781, ((0, 32), (2, 8))),
        "adapter_up_key_value": normal_values(streams_of[9], (ADAPTER_POOL, 2, ADAPTER_RANK, KEY_VALUE_HEADS * HEAD_SIZE), 0.04, 0.23925781, ((0, 32), (3, 8))),
        "adapter_up_output": normal_values(streams_of[10], (ADAPTER_POOL, ADAPTER_RANK, MODEL_WIDTH), 0.12, 0.71875, ((0, 32), (2, 8))),
    }


adapter_scale = 2.0
rope_base = 500000.0

def layout(lengths_row, token_total):
    end_points = jnp.cumsum(lengths_row)
    request_starts = end_points - lengths_row
    positions = jnp.arange(token_total, dtype=jnp.int32)
    owning_request = lax.optimization_barrier(jnp.sum((positions[:, None] >= end_points[None, :]).astype(jnp.int32), axis=1))
    matches = owning_request[:, None] == jnp.arange(lengths_row.shape[0], dtype=jnp.int32)[None, :]
    offsets = lax.optimization_barrier(jnp.sum(jnp.where(matches, request_starts[None, :], 0), axis=1))
    return (request_starts, owning_request, positions - offsets)

def rope_tables(positions, head_dim):
    half_dim = head_dim // 2
    frequency = jnp.power(rope_base, -jnp.arange(half_dim, dtype=jnp.float32) * (2.0 / head_dim))
    angles = positions.astype(jnp.float32)[:, None] * frequency[None, :]
    return (jnp.cos(angles), jnp.sin(angles))

def rotate_halves(values, cosine_values, sine_values):
    half_dim = values.shape[-1] // 2
    first_half = values[..., :half_dim]
    second_half = values[..., half_dim:]
    cosines = cosine_values[:, None, :]
    sine_rows = sine_values[:, None, :]
    return jnp.concatenate([first_half * cosines - second_half * sine_rows, second_half * cosines + first_half * sine_rows], axis=-1)

def segment_mask(inputs, weights, request_starts, owning_request, longest):
    token_total = inputs.shape[0]

    def add_request(running, element):
        weight, start_row, request_index = element
        first_row = jnp.clip(start_row, 0, token_total - longest).astype(jnp.int32)
        block_rows = lax.dynamic_slice_in_dim(inputs, first_row, longest, 0)
        product = jnp.dot(block_rows, weight, preferred_element_type=jnp.float32)
        inside = lax.dynamic_slice_in_dim(owning_request, first_row, longest, 0) == request_index
        current = lax.dynamic_slice_in_dim(running, first_row, longest, 0)
        running = lax.dynamic_update_slice_in_dim(running, current + jnp.where(inside[:, None], product, 0.0), first_row, 0)
        return (running, None)
    initial = jnp.zeros((token_total, weights.shape[2]), jnp.float32)
    indices = jnp.arange(weights.shape[0], dtype=jnp.int32)
    result, unused = lax.scan(add_request, initial, (weights, request_starts, indices))
    return result

def attend_group(query_rows, key_head_rows, value_head_rows, owning_request):
    token_total = query_rows.shape[0]
    block_size = min(512, token_total)
    positions = jnp.arange(token_total, dtype=jnp.int32)

    def one_block(block_index):
        first_row = block_index * block_size
        query_block = lax.dynamic_slice_in_dim(query_rows, first_row, block_size, 0)
        own_request = lax.dynamic_slice_in_dim(owning_request, first_row, block_size, 0)
        own_position = first_row + jnp.arange(block_size, dtype=jnp.int32)
        allowed = (own_request[:, None] == owning_request[None, :]) & (positions[None, :] <= own_position[:, None])
        scores = jnp.einsum('qhgd,khd->hgqk', query_block.astype(jnp.float32), key_head_rows.astype(jnp.float32)) / math.sqrt(HEAD_SIZE)
        scores = jnp.where(allowed[None, None], scores, -jnp.inf)
        row_top = lax.optimization_barrier(jnp.max(scores, axis=-1, keepdims=True))
        weights = jnp.exp(scores - row_top)
        probabilities = (weights / lax.optimization_barrier(jnp.sum(weights, axis=-1, keepdims=True))).astype(jnp.bfloat16)
        mixed = jnp.einsum('hgqk,khd->qhgd', probabilities.astype(jnp.float32), value_head_rows.astype(jnp.float32))
        return mixed.astype(jnp.bfloat16)
    blocks = lax.map(one_block, jnp.arange(token_total // block_size, dtype=jnp.int32))
    return blocks.reshape(token_total, -1)

def reference(hidden, base_query_weight, base_key_weight, base_value_weight, lengths, request_adapter, adapter_pool_row, adapter_down_weight, adapter_up_query, adapter_up_key_value, adapter_up_output):
    pool_rows = adapter_pool_row[request_adapter]
    group_length = QUERY_HEADS // KEY_VALUE_HEADS

    def one_group(element):
        group_hidden, group_query_rows, group_key_rows, group_value_rows, group_lengths, group_token_rows = element
        down_weight_panels = adapter_down_weight[group_token_rows]
        query_up_weight = adapter_up_query[group_token_rows]
        key_value_up_weight = adapter_up_key_value[group_token_rows]
        output_up_weight = adapter_up_output[group_token_rows]
        request_starts, owning_request, positions = layout(group_lengths, GROUP_TOKENS)
        ranks = segment_mask(group_hidden, down_weight_panels[:, :, :3 * ADAPTER_RANK], request_starts, owning_request, LONGEST_REQUEST).astype(jnp.bfloat16)
        query_delta = segment_mask(ranks[:, :ADAPTER_RANK], query_up_weight, request_starts, owning_request, LONGEST_REQUEST)
        key_delta = segment_mask(ranks[:, ADAPTER_RANK:2 * ADAPTER_RANK], key_value_up_weight[:, 0], request_starts, owning_request, LONGEST_REQUEST)
        value_delta = segment_mask(ranks[:, 2 * ADAPTER_RANK:], key_value_up_weight[:, 1], request_starts, owning_request, LONGEST_REQUEST)
        cosine_values, sine_values = rope_tables(positions, HEAD_SIZE)
        query_rows = rotate_halves((group_query_rows.astype(jnp.float32) + adapter_scale * query_delta).reshape(GROUP_TOKENS, QUERY_HEADS, HEAD_SIZE), cosine_values, sine_values).astype(jnp.bfloat16)
        rotated_keys = rotate_halves((group_key_rows.astype(jnp.float32) + adapter_scale * key_delta).reshape(GROUP_TOKENS, KEY_VALUE_HEADS, HEAD_SIZE), cosine_values, sine_values).astype(jnp.bfloat16)
        input_values = (group_value_rows.astype(jnp.float32) + adapter_scale * value_delta).astype(jnp.bfloat16).reshape(GROUP_TOKENS, KEY_VALUE_HEADS, HEAD_SIZE)
        context = attend_group(query_rows.reshape(GROUP_TOKENS, KEY_VALUE_HEADS, group_length, HEAD_SIZE), rotated_keys, input_values, owning_request)
        output_ranks = segment_mask(context, down_weight_panels[:, :, 3 * ADAPTER_RANK:], request_starts, owning_request, LONGEST_REQUEST).astype(jnp.bfloat16)
        adapter_choice = (adapter_scale * segment_mask(output_ranks, output_up_weight, request_starts, owning_request, LONGEST_REQUEST)).astype(jnp.bfloat16)
        return (context, adapter_choice)
    context, adapter_out = lax.map(one_group, (hidden, base_query_weight, base_key_weight, base_value_weight, lengths, pool_rows))
    return (context, adapter_out)
```

```python
import math

import jax
import jax.numpy as jnp
from jax import lax
from jax.sharding import PartitionSpec as P

HEAD_SIZE = 128


adapter_scale = 2.0
rope_base = 500000.0


def layout(lengths_row, token_total):
    end_points = jnp.cumsum(lengths_row)
    request_starts = end_points - lengths_row
    positions = jnp.arange(token_total, dtype=jnp.int32)
    owning_request = jnp.sum((positions[:, None] >= end_points[None, :]).astype(jnp.int32), axis=1)
    matches = owning_request[:, None] == jnp.arange(lengths_row.shape[0], dtype=jnp.int32)[None, :]
    offsets = jnp.sum(jnp.where(matches, request_starts[None, :], 0), axis=1)
    return (request_starts, owning_request, positions - offsets)


def rope_tables(positions, head_dim):
    half_dim = head_dim // 2
    frequency = jnp.power(rope_base, -jnp.arange(half_dim, dtype=jnp.float32) * (2.0 / head_dim))
    angles = positions.astype(jnp.float32)[:, None] * frequency[None, :]
    return (jnp.cos(angles), jnp.sin(angles))


def rotate_halves(values, cosine_values, sine_values):
    half_dim = values.shape[-1] // 2
    first_half = values[..., :half_dim]
    second_half = values[..., half_dim:]
    cosines = cosine_values[:, None, :]
    sine_rows = sine_values[:, None, :]
    return jnp.concatenate(
        [
            first_half * cosines - second_half * sine_rows,
            second_half * cosines + first_half * sine_rows,
        ],
        axis=-1,
    )


def segment_mask(inputs, weights, request_starts, owning_request, longest):
    token_total = inputs.shape[0]

    def add_request(running, element):
        weight, start_row, request_index = element
        first_row = jnp.clip(start_row, 0, token_total - longest)
        block_rows = lax.dynamic_slice_in_dim(inputs, first_row, longest, 0)
        product = jnp.dot(block_rows, weight, preferred_element_type=jnp.float32)
        inside = lax.dynamic_slice_in_dim(owning_request, first_row, longest, 0) == request_index
        current = lax.dynamic_slice_in_dim(running, first_row, longest, 0)
        running = lax.dynamic_update_slice_in_dim(
            running, current + jnp.where(inside[:, None], product, 0.0), first_row, 0
        )
        return (running, None)

    initial = jnp.zeros((token_total, weights.shape[2]), jnp.float32)
    indices = jnp.arange(weights.shape[0], dtype=jnp.int32)
    result, unused = lax.scan(add_request, initial, (weights, request_starts, indices))
    return result


def attend_group(query_rows, key_head_rows, value_head_rows, owning_request):
    token_total = query_rows.shape[0]
    block_size = min(512, token_total)
    positions = jnp.arange(token_total, dtype=jnp.int32)

    def one_block(block_index):
        first_row = block_index * block_size
        query_block = lax.dynamic_slice_in_dim(query_rows, first_row, block_size, 0)
        own_request = lax.dynamic_slice_in_dim(owning_request, first_row, block_size, 0)
        own_position = first_row + jnp.arange(block_size, dtype=jnp.int32)
        allowed = (own_request[:, None] == owning_request[None, :]) & (
            positions[None, :] <= own_position[:, None]
        )
        scores = jnp.einsum(
            "qhgd,khd->hgqk", query_block, key_head_rows, preferred_element_type=jnp.float32
        ) / math.sqrt(HEAD_SIZE)
        scores = jnp.where(allowed[None, None], scores, -jnp.inf)
        row_top = jnp.max(scores, axis=-1, keepdims=True)
        weights = jnp.exp(scores - row_top)
        probabilities = (weights / jnp.sum(weights, axis=-1, keepdims=True)).astype(jnp.bfloat16)
        mixed = jnp.einsum(
            "hgqk,khd->qhgd", probabilities, value_head_rows, preferred_element_type=jnp.float32
        )
        return mixed.astype(jnp.bfloat16)

    blocks = lax.map(one_block, jnp.arange(token_total // block_size, dtype=jnp.int32))
    return blocks.reshape(token_total, -1)


def attend_banded(query_rows, key_head_rows, value_head_rows, owning_request, longest):
    token_total = query_rows.shape[0]
    block_size = min(256, token_total)
    blocks = []
    for block_index in range(token_total // block_size):
        first_row = block_index * block_size
        first_key = max(0, first_row - longest)
        last_key = first_row + block_size
        query_block = query_rows[first_row:last_key]
        key_block = key_head_rows[first_key:last_key]
        value_block = value_head_rows[first_key:last_key]
        own_request = owning_request[first_row:last_key]
        key_request = owning_request[first_key:last_key]
        own_position = first_row + jnp.arange(block_size, dtype=jnp.int32)
        key_position = first_key + jnp.arange(last_key - first_key, dtype=jnp.int32)
        allowed = (own_request[:, None] == key_request[None, :]) & (
            key_position[None, :] <= own_position[:, None]
        )
        scores = jnp.einsum(
            "qhgd,khd->hgqk", query_block, key_block, preferred_element_type=jnp.float32
        ) / math.sqrt(HEAD_SIZE)
        scores = jnp.where(allowed[None, None], scores, -jnp.inf)
        row_top = jnp.max(scores, axis=-1, keepdims=True)
        weights = jnp.exp(scores - row_top)
        probabilities = (weights / jnp.sum(weights, axis=-1, keepdims=True)).astype(jnp.bfloat16)
        mixed = jnp.einsum(
            "hgqk,khd->qhgd", probabilities, value_block, preferred_element_type=jnp.float32
        )
        blocks.append(mixed.astype(jnp.bfloat16).reshape(block_size, -1))
    return jnp.concatenate(blocks, axis=0)


def body(
    hidden,
    base_query_weight,
    base_key_weight,
    base_value_weight,
    lengths,
    request_adapter,
    adapter_pool_row,
    adapter_down_weight,
    adapter_up_query,
    adapter_up_key_value,
    adapter_up_output,
):
    group_count = lax.axis_size("dp")
    seq_count = lax.axis_size("seq")
    my_group = lax.axis_index("dp")
    my_seat = lax.axis_index("seq")
    local_pool_rows = adapter_down_weight.shape[0]
    requests = request_adapter.shape[1]
    capacity = (2 * requests + group_count - 1) // group_count
    rank_width = adapter_up_query.shape[1]
    adapter_count = adapter_pool_row.shape[0]
    matches = (
        request_adapter[:, :, None] == jnp.arange(adapter_count, dtype=jnp.int32)[None, None, :]
    )
    pool_rows = jnp.sum(jnp.where(matches, adapter_pool_row[None, None, :], 0), axis=2)
    owners = pool_rows // local_pool_rows
    local_slot = pool_rows % local_pool_rows
    owned_here = owners == my_group
    slot_index = jnp.cumsum(owned_here.astype(jnp.int32), axis=1) - 1
    capacity_range = jnp.arange(capacity, dtype=jnp.int32)
    local_range = jnp.arange(local_pool_rows, dtype=jnp.int32)
    chosen = (
        owned_here[:, :, None, None]
        & (slot_index[:, :, None, None] == capacity_range[None, None, :, None])
        & (local_slot[:, :, None, None] == local_range[None, None, None, :])
    )
    selection = (
        jnp.sum(chosen.astype(jnp.float32), axis=1)
        .astype(jnp.bfloat16)
        .reshape(group_count * capacity, local_pool_rows)
    )

    def selected_rows(pool_table):
        flattened = pool_table.reshape(local_pool_rows, -1)
        picked = jnp.dot(selection, flattened, preferred_element_type=jnp.float32).astype(
            jnp.bfloat16
        )
        return picked.reshape((group_count * capacity,) + pool_table.shape[1:])

    group_token_rows = lax.dynamic_index_in_dim(pool_rows, my_group, 0, keepdims=False)
    group_owner = group_token_rows // local_pool_rows
    request_range = jnp.arange(requests, dtype=jnp.int32)
    earlier = request_range[None, :] < request_range[:, None]
    same_owner = group_owner[None, :] == group_owner[:, None]
    order_in_owner = jnp.sum((earlier & same_owner).astype(jnp.int32), axis=1)
    arrival = group_owner * capacity + order_in_owner
    received = (
        lax.all_to_all(
            selected_rows(adapter_down_weight), "dp", split_axis=0, concat_axis=0, tiled=True
        ),
        lax.all_to_all(
            selected_rows(adapter_up_query), "dp", split_axis=0, concat_axis=0, tiled=True
        ),
        lax.all_to_all(
            selected_rows(adapter_up_key_value), "dp", split_axis=0, concat_axis=0, tiled=True
        ),
        lax.all_to_all(
            selected_rows(adapter_up_output), "dp", split_axis=0, concat_axis=0, tiled=True
        ),
    )
    fetched_o = jnp.take(received[3], arrival, axis=0)
    fetched_down = jnp.take(received[0], arrival, axis=0)
    fetched_q = jnp.take(received[1], arrival, axis=0)
    fetched_kv = jnp.take(received[2], arrival, axis=0)
    tokens_here = hidden.shape[1]
    token_total = tokens_here * seq_count
    longest = token_total // 4
    request_starts, owning_request, positions = layout(lengths[0], token_total)
    features, query_head_rows, key_head_rows, value_head_rows = (
        lax.all_to_all(hidden[0], "seq", split_axis=1, concat_axis=0, tiled=True),
        lax.all_to_all(base_query_weight[0], "seq", split_axis=1, concat_axis=0, tiled=True),
        lax.all_to_all(base_key_weight[0], "seq", split_axis=1, concat_axis=0, tiled=True),
        lax.all_to_all(base_value_weight[0], "seq", split_axis=1, concat_axis=0, tiled=True),
    )
    request_hot = (owning_request[:, None] == request_range[None, :])
    hot_f32 = request_hot.astype(jnp.float32)
    hot_bf16 = request_hot.astype(jnp.bfloat16)

    def down_select(inputs, panels):
        product = jnp.einsum("tf,rfc->trc", inputs, panels, preferred_element_type=jnp.float32)
        return jnp.sum(product * hot_f32[:, :, None], axis=1)

    def up_spread(rank_rows, panels):
        spread = (hot_bf16[:, :, None] * rank_rows[:, None, :]).reshape(token_total, -1)
        return jnp.dot(
            spread, panels.reshape(-1, panels.shape[-1]), preferred_element_type=jnp.float32
        )

    rank_terms = down_select(features, fetched_down[:, :, : 3 * rank_width])
    ranks = lax.psum(rank_terms, "seq").astype(jnp.bfloat16)
    query_delta = up_spread(ranks[:, :rank_width], fetched_q)
    key_delta = up_spread(ranks[:, rank_width : 2 * rank_width], fetched_kv[:, 0])
    value_delta = up_spread(ranks[:, 2 * rank_width :], fetched_kv[:, 1])
    query_local = query_head_rows.shape[1] // HEAD_SIZE
    local_key_value = key_head_rows.shape[1] // HEAD_SIZE
    group_length = query_local // local_key_value
    cosine_values, sine_values = rope_tables(positions, HEAD_SIZE)
    query_rows = rotate_halves(
        (query_head_rows.astype(jnp.float32) + adapter_scale * query_delta).reshape(
            token_total, query_local, HEAD_SIZE
        ),
        cosine_values,
        sine_values,
    ).astype(jnp.bfloat16)
    rotated_keys = rotate_halves(
        (key_head_rows.astype(jnp.float32) + adapter_scale * key_delta).reshape(
            token_total, local_key_value, HEAD_SIZE
        ),
        cosine_values,
        sine_values,
    ).astype(jnp.bfloat16)
    input_values = (
        (value_head_rows.astype(jnp.float32) + adapter_scale * value_delta)
        .astype(jnp.bfloat16)
        .reshape(token_total, local_key_value, HEAD_SIZE)
    )
    context = attend_banded(
        query_rows.reshape(token_total, local_key_value, group_length, HEAD_SIZE),
        rotated_keys,
        input_values,
        owning_request,
        longest,
    )
    rank_terms_o = down_select(context, fetched_down[:, :, 3 * rank_width :])
    context_rows = lax.all_to_all(context, "seq", split_axis=0, concat_axis=1, tiled=True)
    output_ranks = lax.psum_scatter(
        rank_terms_o.astype(jnp.bfloat16), "seq", scatter_dimension=0, tiled=True
    )
    up_full = lax.all_gather(fetched_o, "seq", axis=2, tiled=True)
    my_requests = lax.dynamic_slice_in_dim(owning_request, my_seat * tokens_here, tokens_here, 0)
    onehot = (my_requests[:, None] == request_range[None, :]).astype(jnp.bfloat16)
    spread = (onehot[:, :, None] * output_ranks[:, None, :]).reshape(
        tokens_here, requests * rank_width
    )
    adapter_rows = (
        adapter_scale
        * jnp.dot(
            spread, up_full.reshape(requests * rank_width, -1), preferred_element_type=jnp.float32
        )
    ).astype(jnp.bfloat16)
    return (context_rows[None], adapter_rows[None])


def solution(mesh):
    placed = (
        P("dp", "seq", None),
        P("dp", "seq", None),
        P("dp", "seq", None),
        P("dp", "seq", None),
        P("dp", None),
        P(),
        P(),
        P("dp", "seq", None),
        P("dp", None, "seq"),
        P("dp", None, None, "seq"),
        P("dp", None, "seq"),
    )
    return jax.shard_map(
        body,
        mesh=mesh,
        in_specs=placed,
        out_specs=(P("dp", "seq", None), P("dp", "seq", None)),
        check_vma=False,
    )
```

```python
import math

import jax
import jax.numpy as jnp
from jax import lax
from jax.sharding import PartitionSpec as P

HEAD_SIZE = 128


adapter_scale = 2.0
rope_base = 500000.0


def layout(lengths_row, token_total):
    end_points = jnp.cumsum(lengths_row)
    request_starts = end_points - lengths_row
    positions = jnp.arange(token_total, dtype=jnp.int32)
    owning_request = jnp.sum((positions[:, None] >= end_points[None, :]).astype(jnp.int32), axis=1)
    matches = owning_request[:, None] == jnp.arange(lengths_row.shape[0], dtype=jnp.int32)[None, :]
    offsets = jnp.sum(jnp.where(matches, request_starts[None, :], 0), axis=1)
    return (request_starts, owning_request, positions - offsets)


def rope_tables(positions, head_dim):
    half_dim = head_dim // 2
    frequency = jnp.power(rope_base, -jnp.arange(half_dim, dtype=jnp.float32) * (2.0 / head_dim))
    angles = positions.astype(jnp.float32)[:, None] * frequency[None, :]
    return (jnp.cos(angles), jnp.sin(angles))


def rotate_halves(values, cosine_values, sine_values):
    half_dim = values.shape[-1] // 2
    first_half = values[..., :half_dim]
    second_half = values[..., half_dim:]
    cosines = cosine_values[:, None, :]
    sine_rows = sine_values[:, None, :]
    return jnp.concatenate(
        [
            first_half * cosines - second_half * sine_rows,
            second_half * cosines + first_half * sine_rows,
        ],
        axis=-1,
    )


def segment_mask(inputs, weights, request_starts, owning_request, longest):
    token_total = inputs.shape[0]

    def add_request(running, element):
        weight, start_row, request_index = element
        first_row = jnp.clip(start_row, 0, token_total - longest)
        block_rows = lax.dynamic_slice_in_dim(inputs, first_row, longest, 0)
        product = jnp.dot(block_rows, weight, preferred_element_type=jnp.float32)
        inside = lax.dynamic_slice_in_dim(owning_request, first_row, longest, 0) == request_index
        current = lax.dynamic_slice_in_dim(running, first_row, longest, 0)
        running = lax.dynamic_update_slice_in_dim(
            running, current + jnp.where(inside[:, None], product, 0.0), first_row, 0
        )
        return (running, None)

    initial = jnp.zeros((token_total, weights.shape[2]), jnp.float32)
    indices = jnp.arange(weights.shape[0], dtype=jnp.int32)
    result, unused = lax.scan(add_request, initial, (weights, request_starts, indices))
    return result


def attend_group(query_rows, key_head_rows, value_head_rows, owning_request):
    token_total = query_rows.shape[0]
    block_size = min(512, token_total)
    positions = jnp.arange(token_total, dtype=jnp.int32)

    def one_block(block_index):
        first_row = block_index * block_size
        query_block = lax.dynamic_slice_in_dim(query_rows, first_row, block_size, 0)
        own_request = lax.dynamic_slice_in_dim(owning_request, first_row, block_size, 0)
        own_position = first_row + jnp.arange(block_size, dtype=jnp.int32)
        allowed = (own_request[:, None] == owning_request[None, :]) & (
            positions[None, :] <= own_position[:, None]
        )
        scores = jnp.einsum(
            "qhgd,khd->hgqk", query_block, key_head_rows, preferred_element_type=jnp.float32
        ) / math.sqrt(HEAD_SIZE)
        scores = jnp.where(allowed[None, None], scores, -jnp.inf)
        row_top = jnp.max(scores, axis=-1, keepdims=True)
        weights = jnp.exp(scores - row_top)
        probabilities = (weights / jnp.sum(weights, axis=-1, keepdims=True)).astype(jnp.bfloat16)
        mixed = jnp.einsum(
            "hgqk,khd->qhgd", probabilities, value_head_rows, preferred_element_type=jnp.float32
        )
        return mixed.astype(jnp.bfloat16)

    blocks = lax.map(one_block, jnp.arange(token_total // block_size, dtype=jnp.int32))
    return blocks.reshape(token_total, -1)


def attend_banded(query_rows, key_head_rows, value_head_rows, owning_request, longest):
    token_total = query_rows.shape[0]
    block_size = min(256, token_total)
    blocks = []
    for block_index in range(token_total // block_size):
        first_row = block_index * block_size
        first_key = max(0, first_row - longest)
        last_key = first_row + block_size
        query_block = query_rows[first_row:last_key]
        key_block = key_head_rows[first_key:last_key]
        value_block = value_head_rows[first_key:last_key]
        own_request = owning_request[first_row:last_key]
        key_request = owning_request[first_key:last_key]
        own_position = first_row + jnp.arange(block_size, dtype=jnp.int32)
        key_position = first_key + jnp.arange(last_key - first_key, dtype=jnp.int32)
        allowed = (own_request[:, None] == key_request[None, :]) & (
            key_position[None, :] <= own_position[:, None]
        )
        scores = jnp.einsum(
            "qhgd,khd->hgqk", query_block, key_block, preferred_element_type=jnp.float32
        ) / math.sqrt(HEAD_SIZE)
        scores = jnp.where(allowed[None, None], scores, -jnp.inf)
        row_top = jnp.max(scores, axis=-1, keepdims=True)
        weights = jnp.exp(scores - row_top)
        probabilities = (weights / jnp.sum(weights, axis=-1, keepdims=True)).astype(jnp.bfloat16)
        mixed = jnp.einsum(
            "hgqk,khd->qhgd", probabilities, value_block, preferred_element_type=jnp.float32
        )
        blocks.append(mixed.astype(jnp.bfloat16).reshape(block_size, -1))
    return jnp.concatenate(blocks, axis=0)


def body(
    hidden,
    base_query_weight,
    base_key_weight,
    base_value_weight,
    lengths,
    request_adapter,
    adapter_pool_row,
    adapter_down_weight,
    adapter_up_query,
    adapter_up_key_value,
    adapter_up_output,
):
    group_count = lax.axis_size("dp")
    seq_count = lax.axis_size("seq")
    my_group = lax.axis_index("dp")
    my_seat = lax.axis_index("seq")
    local_pool_rows = adapter_down_weight.shape[0]
    requests = request_adapter.shape[1]
    capacity = (2 * requests + group_count - 1) // group_count
    rank_width = adapter_up_query.shape[1]
    adapter_count = adapter_pool_row.shape[0]
    matches = (
        request_adapter[:, :, None] == jnp.arange(adapter_count, dtype=jnp.int32)[None, None, :]
    )
    pool_rows = jnp.sum(jnp.where(matches, adapter_pool_row[None, None, :], 0), axis=2)
    owners = pool_rows // local_pool_rows
    local_slot = pool_rows % local_pool_rows
    owned_here = owners == my_group
    slot_index = jnp.cumsum(owned_here.astype(jnp.int32), axis=1) - 1
    capacity_range = jnp.arange(capacity, dtype=jnp.int32)
    local_range = jnp.arange(local_pool_rows, dtype=jnp.int32)
    chosen = (
        owned_here[:, :, None, None]
        & (slot_index[:, :, None, None] == capacity_range[None, None, :, None])
        & (local_slot[:, :, None, None] == local_range[None, None, None, :])
    )
    selection = (
        jnp.sum(chosen.astype(jnp.float32), axis=1)
        .astype(jnp.bfloat16)
        .reshape(group_count * capacity, local_pool_rows)
    )

    def selected_rows(pool_table):
        flattened = pool_table.reshape(local_pool_rows, -1)
        picked = jnp.dot(selection, flattened, preferred_element_type=jnp.float32).astype(
            jnp.bfloat16
        )
        return picked.reshape((group_count * capacity,) + pool_table.shape[1:])

    group_token_rows = lax.dynamic_index_in_dim(pool_rows, my_group, 0, keepdims=False)
    group_owner = group_token_rows // local_pool_rows
    request_range = jnp.arange(requests, dtype=jnp.int32)
    earlier = request_range[None, :] < request_range[:, None]
    same_owner = group_owner[None, :] == group_owner[:, None]
    order_in_owner = jnp.sum((earlier & same_owner).astype(jnp.int32), axis=1)
    arrival = group_owner * capacity + order_in_owner
    down_panels = selected_rows(adapter_down_weight)
    received_down = lax.all_to_all(
        down_panels[:, :, : 3 * rank_width], "dp", split_axis=0, concat_axis=0, tiled=True
    )
    received_q = lax.all_to_all(
        selected_rows(adapter_up_query), "dp", split_axis=0, concat_axis=0, tiled=True
    )
    received_kv = lax.all_to_all(
        selected_rows(adapter_up_key_value), "dp", split_axis=0, concat_axis=0, tiled=True
    )
    received_down_o = lax.all_to_all(
        down_panels[:, :, 3 * rank_width :], "dp", split_axis=0, concat_axis=0, tiled=True
    )
    received_o = lax.all_to_all(
        selected_rows(adapter_up_output), "dp", split_axis=0, concat_axis=0, tiled=True
    )
    fetched_o = jnp.take(received_o, arrival, axis=0)
    fetched_down = jnp.take(received_down, arrival, axis=0)
    fetched_down_o = jnp.take(received_down_o, arrival, axis=0)
    fetched_q = jnp.take(received_q, arrival, axis=0)
    fetched_kv = jnp.take(received_kv, arrival, axis=0)
    tokens_here = hidden.shape[1]
    token_total = tokens_here * seq_count
    longest = token_total // 4
    request_starts, owning_request, positions = layout(lengths[0], token_total)
    features, query_head_rows, key_head_rows, value_head_rows = (
        lax.all_to_all(hidden[0], "seq", split_axis=1, concat_axis=0, tiled=True),
        lax.all_to_all(base_query_weight[0], "seq", split_axis=1, concat_axis=0, tiled=True),
        lax.all_to_all(base_key_weight[0], "seq", split_axis=1, concat_axis=0, tiled=True),
        lax.all_to_all(base_value_weight[0], "seq", split_axis=1, concat_axis=0, tiled=True),
    )
    request_hot = (owning_request[:, None] == request_range[None, :])
    hot_f32 = request_hot.astype(jnp.float32)
    hot_bf16 = request_hot.astype(jnp.bfloat16)

    def down_select(inputs, panels):
        product = jnp.einsum("tf,rfc->trc", inputs, panels, preferred_element_type=jnp.float32)
        return jnp.sum(product * hot_f32[:, :, None], axis=1)

    def up_spread(rank_rows, panels):
        spread = (hot_bf16[:, :, None] * rank_rows[:, None, :]).reshape(token_total, -1)
        return jnp.dot(
            spread, panels.reshape(-1, panels.shape[-1]), preferred_element_type=jnp.float32
        )

    rank_terms = down_select(features, fetched_down)
    rank_shard = lax.psum_scatter(rank_terms, "seq", scatter_dimension=0, tiled=True)
    ranks = lax.all_gather(rank_shard.astype(jnp.bfloat16), "seq", axis=0, tiled=True)
    query_delta = up_spread(ranks[:, :rank_width], fetched_q)
    key_delta = up_spread(ranks[:, rank_width : 2 * rank_width], fetched_kv[:, 0])
    value_delta = up_spread(ranks[:, 2 * rank_width :], fetched_kv[:, 1])
    query_local = query_head_rows.shape[1] // HEAD_SIZE
    local_key_value = key_head_rows.shape[1] // HEAD_SIZE
    group_length = query_local // local_key_value
    cosine_values, sine_values = rope_tables(positions, HEAD_SIZE)
    query_rows = rotate_halves(
        (query_head_rows.astype(jnp.float32) + adapter_scale * query_delta).reshape(
            token_total, query_local, HEAD_SIZE
        ),
        cosine_values,
        sine_values,
    ).astype(jnp.bfloat16)
    rotated_keys = rotate_halves(
        (key_head_rows.astype(jnp.float32) + adapter_scale * key_delta).reshape(
            token_total, local_key_value, HEAD_SIZE
        ),
        cosine_values,
        sine_values,
    ).astype(jnp.bfloat16)
    input_values = (
        (value_head_rows.astype(jnp.float32) + adapter_scale * value_delta)
        .astype(jnp.bfloat16)
        .reshape(token_total, local_key_value, HEAD_SIZE)
    )
    context = attend_banded(
        query_rows.reshape(token_total, local_key_value, group_length, HEAD_SIZE),
        rotated_keys,
        input_values,
        owning_request,
        longest,
    )
    rank_terms_o = down_select(context, fetched_down_o)
    context_rows = lax.all_to_all(context, "seq", split_axis=0, concat_axis=1, tiled=True)
    output_ranks = lax.psum_scatter(
        rank_terms_o.astype(jnp.bfloat16), "seq", scatter_dimension=0, tiled=True
    )
    up_full = lax.all_gather(fetched_o, "seq", axis=2, tiled=True)
    my_requests = lax.dynamic_slice_in_dim(owning_request, my_seat * tokens_here, tokens_here, 0)
    onehot = (my_requests[:, None] == request_range[None, :]).astype(jnp.bfloat16)
    spread = (onehot[:, :, None] * output_ranks[:, None, :]).reshape(
        tokens_here, requests * rank_width
    )
    adapter_rows = (
        adapter_scale
        * jnp.dot(
            spread, up_full.reshape(requests * rank_width, -1), preferred_element_type=jnp.float32
        )
    ).astype(jnp.bfloat16)
    return (context_rows[None], adapter_rows[None])


def solution(mesh):
    placed = (
        P("dp", "seq", None),
        P("dp", "seq", None),
        P("dp", "seq", None),
        P("dp", "seq", None),
        P("dp", None),
        P(),
        P(),
        P("dp", "seq", None),
        P("dp", None, "seq"),
        P("dp", None, None, "seq"),
        P("dp", None, "seq"),
    )
    return jax.shard_map(
        body,
        mesh=mesh,
        in_specs=placed,
        out_specs=(P("dp", "seq", None), P("dp", "seq", None)),
        check_vma=False,
    )
```

```python
import math

import jax
import jax.numpy as jnp
from jax import lax
from jax.sharding import PartitionSpec as P

HEAD_SIZE = 128


adapter_scale = 2.0
rope_base = 500000.0


def layout(lengths_row, token_total):
    end_points = jnp.cumsum(lengths_row)
    request_starts = end_points - lengths_row
    positions = jnp.arange(token_total, dtype=jnp.int32)
    owning_request = jnp.sum((positions[:, None] >= end_points[None, :]).astype(jnp.int32), axis=1)
    matches = owning_request[:, None] == jnp.arange(lengths_row.shape[0], dtype=jnp.int32)[None, :]
    offsets = jnp.sum(jnp.where(matches, request_starts[None, :], 0), axis=1)
    return (request_starts, owning_request, positions - offsets)


def rope_tables(positions, head_dim):
    half_dim = head_dim // 2
    frequency = jnp.power(rope_base, -jnp.arange(half_dim, dtype=jnp.float32) * (2.0 / head_dim))
    angles = positions.astype(jnp.float32)[:, None] * frequency[None, :]
    return (jnp.cos(angles), jnp.sin(angles))


def rotate_halves(values, cosine_values, sine_values):
    half_dim = values.shape[-1] // 2
    first_half = values[..., :half_dim]
    second_half = values[..., half_dim:]
    cosines = cosine_values[:, None, :]
    sine_rows = sine_values[:, None, :]
    return jnp.concatenate(
        [
            first_half * cosines - second_half * sine_rows,
            second_half * cosines + first_half * sine_rows,
        ],
        axis=-1,
    )


def segment_mask(inputs, weights, request_starts, owning_request, longest):
    token_total = inputs.shape[0]

    def add_request(running, element):
        weight, start_row, request_index = element
        first_row = jnp.clip(start_row, 0, token_total - longest)
        block_rows = lax.dynamic_slice_in_dim(inputs, first_row, longest, 0)
        product = jnp.dot(block_rows, weight, preferred_element_type=jnp.float32)
        inside = lax.dynamic_slice_in_dim(owning_request, first_row, longest, 0) == request_index
        current = lax.dynamic_slice_in_dim(running, first_row, longest, 0)
        running = lax.dynamic_update_slice_in_dim(
            running, current + jnp.where(inside[:, None], product, 0.0), first_row, 0
        )
        return (running, None)

    initial = jnp.zeros((token_total, weights.shape[2]), jnp.float32)
    indices = jnp.arange(weights.shape[0], dtype=jnp.int32)
    result, unused = lax.scan(add_request, initial, (weights, request_starts, indices))
    return result


def attend_group(query_rows, key_head_rows, value_head_rows, owning_request):
    token_total = query_rows.shape[0]
    block_size = min(512, token_total)
    positions = jnp.arange(token_total, dtype=jnp.int32)

    def one_block(block_index):
        first_row = block_index * block_size
        query_block = lax.dynamic_slice_in_dim(query_rows, first_row, block_size, 0)
        own_request = lax.dynamic_slice_in_dim(owning_request, first_row, block_size, 0)
        own_position = first_row + jnp.arange(block_size, dtype=jnp.int32)
        allowed = (own_request[:, None] == owning_request[None, :]) & (
            positions[None, :] <= own_position[:, None]
        )
        scores = jnp.einsum(
            "qhgd,khd->hgqk", query_block, key_head_rows, preferred_element_type=jnp.float32
        ) / math.sqrt(HEAD_SIZE)
        scores = jnp.where(allowed[None, None], scores, -jnp.inf)
        row_top = jnp.max(scores, axis=-1, keepdims=True)
        weights = jnp.exp(scores - row_top)
        probabilities = (weights / jnp.sum(weights, axis=-1, keepdims=True)).astype(jnp.bfloat16)
        mixed = jnp.einsum(
            "hgqk,khd->qhgd", probabilities, value_head_rows, preferred_element_type=jnp.float32
        )
        return mixed.astype(jnp.bfloat16)

    blocks = lax.map(one_block, jnp.arange(token_total // block_size, dtype=jnp.int32))
    return blocks.reshape(token_total, -1)


def attend_banded(query_rows, key_head_rows, value_head_rows, owning_request, longest):
    token_total = query_rows.shape[0]
    block_size = min(256, token_total)
    blocks = []
    for block_index in range(token_total // block_size):
        first_row = block_index * block_size
        first_key = max(0, first_row - longest)
        last_key = first_row + block_size
        query_block = query_rows[first_row:last_key]
        key_block = key_head_rows[first_key:last_key]
        value_block = value_head_rows[first_key:last_key]
        own_request = owning_request[first_row:last_key]
        key_request = owning_request[first_key:last_key]
        own_position = first_row + jnp.arange(block_size, dtype=jnp.int32)
        key_position = first_key + jnp.arange(last_key - first_key, dtype=jnp.int32)
        allowed = (own_request[:, None] == key_request[None, :]) & (
            key_position[None, :] <= own_position[:, None]
        )
        scores = jnp.einsum(
            "qhgd,khd->hgqk", query_block, key_block, preferred_element_type=jnp.float32
        ) / math.sqrt(HEAD_SIZE)
        scores = jnp.where(allowed[None, None], scores, -jnp.inf)
        row_top = jnp.max(scores, axis=-1, keepdims=True)
        weights = jnp.exp(scores - row_top)
        probabilities = (weights / jnp.sum(weights, axis=-1, keepdims=True)).astype(jnp.bfloat16)
        mixed = jnp.einsum(
            "hgqk,khd->qhgd", probabilities, value_block, preferred_element_type=jnp.float32
        )
        blocks.append(mixed.astype(jnp.bfloat16).reshape(block_size, -1))
    return jnp.concatenate(blocks, axis=0)


def body(
    hidden,
    base_query_weight,
    base_key_weight,
    base_value_weight,
    lengths,
    request_adapter,
    adapter_pool_row,
    adapter_down_weight,
    adapter_up_query,
    adapter_up_key_value,
    adapter_up_output,
):
    group_count = lax.axis_size("dp")
    seq_count = lax.axis_size("seq")
    my_group = lax.axis_index("dp")
    my_seat = lax.axis_index("seq")
    local_pool_rows = adapter_down_weight.shape[0]
    requests = request_adapter.shape[1]
    capacity = (2 * requests + group_count - 1) // group_count
    rank_width = adapter_up_query.shape[1]
    adapter_count = adapter_pool_row.shape[0]
    matches = (
        request_adapter[:, :, None] == jnp.arange(adapter_count, dtype=jnp.int32)[None, None, :]
    )
    pool_rows = jnp.sum(jnp.where(matches, adapter_pool_row[None, None, :], 0), axis=2)
    owners = pool_rows // local_pool_rows
    local_slot = pool_rows % local_pool_rows
    owned_here = owners == my_group
    slot_index = jnp.cumsum(owned_here.astype(jnp.int32), axis=1) - 1
    capacity_range = jnp.arange(capacity, dtype=jnp.int32)
    local_range = jnp.arange(local_pool_rows, dtype=jnp.int32)
    chosen = (
        owned_here[:, :, None, None]
        & (slot_index[:, :, None, None] == capacity_range[None, None, :, None])
        & (local_slot[:, :, None, None] == local_range[None, None, None, :])
    )
    selection = (
        jnp.sum(chosen.astype(jnp.float32), axis=1)
        .astype(jnp.bfloat16)
        .reshape(group_count * capacity, local_pool_rows)
    )

    def selected_rows(pool_table):
        flattened = pool_table.reshape(local_pool_rows, -1)
        picked = jnp.dot(selection, flattened, preferred_element_type=jnp.float32).astype(
            jnp.bfloat16
        )
        return picked.reshape((group_count * capacity,) + pool_table.shape[1:])

    group_token_rows = lax.dynamic_index_in_dim(pool_rows, my_group, 0, keepdims=False)
    group_owner = group_token_rows // local_pool_rows
    request_range = jnp.arange(requests, dtype=jnp.int32)
    earlier = request_range[None, :] < request_range[:, None]
    same_owner = group_owner[None, :] == group_owner[:, None]
    order_in_owner = jnp.sum((earlier & same_owner).astype(jnp.int32), axis=1)
    arrival = group_owner * capacity + order_in_owner
    received_o = lax.all_to_all(
        selected_rows(adapter_up_output), "dp", split_axis=0, concat_axis=0, tiled=True
    )
    down_panels = selected_rows(adapter_down_weight)
    received_down = lax.all_to_all(
        down_panels[:, :, : 3 * rank_width], "dp", split_axis=0, concat_axis=0, tiled=True
    )
    received_q = lax.all_to_all(
        selected_rows(adapter_up_query), "dp", split_axis=0, concat_axis=0, tiled=True
    )
    received_kv = lax.all_to_all(
        selected_rows(adapter_up_key_value), "dp", split_axis=0, concat_axis=0, tiled=True
    )
    fetched_o = jnp.take(received_o, arrival, axis=0)
    fetched_down = jnp.take(received_down, arrival, axis=0)
    fetched_q = jnp.take(received_q, arrival, axis=0)
    fetched_kv = jnp.take(received_kv, arrival, axis=0)
    tokens_here = hidden.shape[1]
    token_total = tokens_here * seq_count
    longest = token_total // 4
    request_starts, owning_request, positions = layout(lengths[0], token_total)
    widths = (
        hidden.shape[2] // seq_count,
        base_query_weight.shape[2] // seq_count,
        base_key_weight.shape[2] // seq_count,
        base_value_weight.shape[2] // seq_count,
    )
    outgoing = jnp.concatenate(
        [
            part[0].reshape(tokens_here, seq_count, width)
            for part, width in zip(
                (hidden, base_query_weight, base_key_weight, base_value_weight), widths
            )
        ],
        axis=2,
    )
    arrived = [lax.dynamic_index_in_dim(outgoing, my_seat, 1, keepdims=False)]
    for shift in range(1, seq_count):
        target = (my_seat + shift) % seq_count
        piece = lax.dynamic_index_in_dim(outgoing, target, 1, keepdims=False)
        arrived.append(
            lax.ppermute(
                piece, "seq", [(i, (i + shift) % seq_count) for i in range(seq_count)]
            )
        )
    arrived = jnp.stack(arrived, axis=0)
    source_order = (my_seat - jnp.arange(seq_count, dtype=jnp.int32)) % seq_count
    gathered = jnp.take(arrived, source_order, axis=0).reshape(token_total, -1)
    edges = [0]
    for width in widths:
        edges.append(edges[-1] + width)
    features, query_head_rows, key_head_rows, value_head_rows = (
        gathered[:, edges[i] : edges[i + 1]] for i in range(4)
    )
    up_full = lax.all_gather(fetched_o, "seq", axis=2, tiled=True)
    up_full, features = lax.optimization_barrier((up_full, features))
    request_hot = (owning_request[:, None] == request_range[None, :])
    hot_f32 = request_hot.astype(jnp.float32)
    hot_bf16 = request_hot.astype(jnp.bfloat16)

    def down_select(inputs, panels):
        product = jnp.einsum("tf,rfc->trc", inputs, panels, preferred_element_type=jnp.float32)
        return jnp.sum(product * hot_f32[:, :, None], axis=1)

    def up_spread(rank_rows, panels):
        spread = (hot_bf16[:, :, None] * rank_rows[:, None, :]).reshape(token_total, -1)
        return jnp.dot(
            spread, panels.reshape(-1, panels.shape[-1]), preferred_element_type=jnp.float32
        )

    rank_terms = down_select(features, fetched_down)
    rank_shard = lax.psum_scatter(rank_terms, "seq", scatter_dimension=0, tiled=True)
    ranks = lax.all_gather(rank_shard.astype(jnp.bfloat16), "seq", axis=0, tiled=True)
    ranks, down_o_panels = lax.optimization_barrier((ranks, down_panels[:, :, 3 * rank_width :]))
    received_down_o = lax.all_to_all(down_o_panels, "dp", split_axis=0, concat_axis=0, tiled=True)
    fetched_down_o = jnp.take(received_down_o, arrival, axis=0)
    query_delta = up_spread(ranks[:, :rank_width], fetched_q)
    key_delta = up_spread(ranks[:, rank_width : 2 * rank_width], fetched_kv[:, 0])
    value_delta = up_spread(ranks[:, 2 * rank_width :], fetched_kv[:, 1])
    query_local = query_head_rows.shape[1] // HEAD_SIZE
    local_key_value = key_head_rows.shape[1] // HEAD_SIZE
    group_length = query_local // local_key_value
    cosine_values, sine_values = rope_tables(positions, HEAD_SIZE)
    query_rows = rotate_halves(
        (query_head_rows.astype(jnp.float32) + adapter_scale * query_delta).reshape(
            token_total, query_local, HEAD_SIZE
        ),
        cosine_values,
        sine_values,
    ).astype(jnp.bfloat16)
    rotated_keys = rotate_halves(
        (key_head_rows.astype(jnp.float32) + adapter_scale * key_delta).reshape(
            token_total, local_key_value, HEAD_SIZE
        ),
        cosine_values,
        sine_values,
    ).astype(jnp.bfloat16)
    input_values = (
        (value_head_rows.astype(jnp.float32) + adapter_scale * value_delta)
        .astype(jnp.bfloat16)
        .reshape(token_total, local_key_value, HEAD_SIZE)
    )
    context = attend_banded(
        query_rows.reshape(token_total, local_key_value, group_length, HEAD_SIZE),
        rotated_keys,
        input_values,
        owning_request,
        longest,
    )
    rank_terms_o = down_select(context, fetched_down_o)
    context_rows = lax.all_to_all(context, "seq", split_axis=0, concat_axis=1, tiled=True)
    output_ranks = lax.psum_scatter(
        rank_terms_o.astype(jnp.bfloat16), "seq", scatter_dimension=0, tiled=True
    )
    my_requests = lax.dynamic_slice_in_dim(owning_request, my_seat * tokens_here, tokens_here, 0)
    onehot = (my_requests[:, None] == request_range[None, :]).astype(jnp.bfloat16)
    spread = (onehot[:, :, None] * output_ranks[:, None, :]).reshape(
        tokens_here, requests * rank_width
    )
    adapter_rows = (
        adapter_scale
        * jnp.dot(
            spread, up_full.reshape(requests * rank_width, -1), preferred_element_type=jnp.float32
        )
    ).astype(jnp.bfloat16)
    return (context_rows[None], adapter_rows[None])


def solution(mesh):
    placed = (
        P("dp", "seq", None),
        P("dp", "seq", None),
        P("dp", "seq", None),
        P("dp", "seq", None),
        P("dp", None),
        P(),
        P(),
        P("dp", "seq", None),
        P("dp", None, "seq"),
        P("dp", None, None, "seq"),
        P("dp", None, "seq"),
    )
    return jax.shard_map(
        body,
        mesh=mesh,
        in_specs=placed,
        out_specs=(P("dp", "seq", None), P("dp", "seq", None)),
        check_vma=False,
    )
```

```python
import math

import jax
import jax.numpy as jnp
from jax import lax
from jax.sharding import PartitionSpec as P

HEAD_SIZE = 128


adapter_scale = 2.0
rope_base = 500000.0


def layout(lengths_row, token_total):
    end_points = jnp.cumsum(lengths_row)
    request_starts = end_points - lengths_row
    positions = jnp.arange(token_total, dtype=jnp.int32)
    owning_request = jnp.sum((positions[:, None] >= end_points[None, :]).astype(jnp.int32), axis=1)
    matches = owning_request[:, None] == jnp.arange(lengths_row.shape[0], dtype=jnp.int32)[None, :]
    offsets = jnp.sum(jnp.where(matches, request_starts[None, :], 0), axis=1)
    return (request_starts, owning_request, positions - offsets)


def rope_tables(positions, head_dim):
    half_dim = head_dim // 2
    frequency = jnp.power(rope_base, -jnp.arange(half_dim, dtype=jnp.float32) * (2.0 / head_dim))
    angles = positions.astype(jnp.float32)[:, None] * frequency[None, :]
    return (jnp.cos(angles), jnp.sin(angles))


def rotate_halves(values, cosine_values, sine_values):
    half_dim = values.shape[-1] // 2
    first_half = values[..., :half_dim]
    second_half = values[..., half_dim:]
    cosines = cosine_values[:, None, :]
    sine_rows = sine_values[:, None, :]
    return jnp.concatenate(
        [
            first_half * cosines - second_half * sine_rows,
            second_half * cosines + first_half * sine_rows,
        ],
        axis=-1,
    )


def segment_mask(inputs, weights, request_starts, owning_request, longest):
    token_total = inputs.shape[0]

    def add_request(running, element):
        weight, start_row, request_index = element
        first_row = jnp.clip(start_row, 0, token_total - longest)
        block_rows = lax.dynamic_slice_in_dim(inputs, first_row, longest, 0)
        product = jnp.dot(block_rows, weight, preferred_element_type=jnp.float32)
        inside = lax.dynamic_slice_in_dim(owning_request, first_row, longest, 0) == request_index
        current = lax.dynamic_slice_in_dim(running, first_row, longest, 0)
        running = lax.dynamic_update_slice_in_dim(
            running, current + jnp.where(inside[:, None], product, 0.0), first_row, 0
        )
        return (running, None)

    initial = jnp.zeros((token_total, weights.shape[2]), jnp.float32)
    indices = jnp.arange(weights.shape[0], dtype=jnp.int32)
    result, unused = lax.scan(add_request, initial, (weights, request_starts, indices))
    return result


def attend_group(query_rows, key_head_rows, value_head_rows, owning_request):
    token_total = query_rows.shape[0]
    block_size = min(512, token_total)
    positions = jnp.arange(token_total, dtype=jnp.int32)

    def one_block(block_index):
        first_row = block_index * block_size
        query_block = lax.dynamic_slice_in_dim(query_rows, first_row, block_size, 0)
        own_request = lax.dynamic_slice_in_dim(owning_request, first_row, block_size, 0)
        own_position = first_row + jnp.arange(block_size, dtype=jnp.int32)
        allowed = (own_request[:, None] == owning_request[None, :]) & (
            positions[None, :] <= own_position[:, None]
        )
        scores = jnp.einsum(
            "qhgd,khd->hgqk", query_block, key_head_rows, preferred_element_type=jnp.float32
        ) / math.sqrt(HEAD_SIZE)
        scores = jnp.where(allowed[None, None], scores, -jnp.inf)
        row_top = jnp.max(scores, axis=-1, keepdims=True)
        weights = jnp.exp(scores - row_top)
        probabilities = (weights / jnp.sum(weights, axis=-1, keepdims=True)).astype(jnp.bfloat16)
        mixed = jnp.einsum(
            "hgqk,khd->qhgd", probabilities, value_head_rows, preferred_element_type=jnp.float32
        )
        return mixed.astype(jnp.bfloat16)

    blocks = lax.map(one_block, jnp.arange(token_total // block_size, dtype=jnp.int32))
    return blocks.reshape(token_total, -1)


def attend_banded(query_rows, key_head_rows, value_head_rows, owning_request, longest, side):
    token_total = query_rows.shape[0]
    block_size = min(256, token_total)
    blocks = []
    block_count = token_total // block_size
    for block_index in range(block_count):
        if block_index == block_count // 2:
            query_rows, side_value = lax.optimization_barrier((query_rows, side()))
        first_row = block_index * block_size
        first_key = max(0, first_row - longest)
        last_key = first_row + block_size
        query_block = query_rows[first_row:last_key]
        key_block = key_head_rows[first_key:last_key]
        value_block = value_head_rows[first_key:last_key]
        own_request = owning_request[first_row:last_key]
        key_request = owning_request[first_key:last_key]
        own_position = first_row + jnp.arange(block_size, dtype=jnp.int32)
        key_position = first_key + jnp.arange(last_key - first_key, dtype=jnp.int32)
        allowed = (own_request[:, None] == key_request[None, :]) & (
            key_position[None, :] <= own_position[:, None]
        )
        scores = jnp.einsum(
            "qhgd,khd->hgqk", query_block, key_block, preferred_element_type=jnp.float32
        ) / math.sqrt(HEAD_SIZE)
        scores = jnp.where(allowed[None, None], scores, -jnp.inf)
        row_top = jnp.max(scores, axis=-1, keepdims=True)
        weights = jnp.exp(scores - row_top)
        probabilities = (weights / jnp.sum(weights, axis=-1, keepdims=True)).astype(jnp.bfloat16)
        mixed = jnp.einsum(
            "hgqk,khd->qhgd", probabilities, value_block, preferred_element_type=jnp.float32
        )
        blocks.append(mixed.astype(jnp.bfloat16).reshape(block_size, -1))
    return jnp.concatenate(blocks, axis=0), side_value


def body(
    hidden,
    base_query_weight,
    base_key_weight,
    base_value_weight,
    lengths,
    request_adapter,
    adapter_pool_row,
    adapter_down_weight,
    adapter_up_query,
    adapter_up_key_value,
    adapter_up_output,
):
    group_count = lax.axis_size("dp")
    seq_count = lax.axis_size("seq")
    my_group = lax.axis_index("dp")
    my_seat = lax.axis_index("seq")
    local_pool_rows = adapter_down_weight.shape[0]
    requests = request_adapter.shape[1]
    capacity = (2 * requests + group_count - 1) // group_count
    rank_width = adapter_up_query.shape[1]
    adapter_count = adapter_pool_row.shape[0]
    matches = (
        request_adapter[:, :, None] == jnp.arange(adapter_count, dtype=jnp.int32)[None, None, :]
    )
    pool_rows = jnp.sum(jnp.where(matches, adapter_pool_row[None, None, :], 0), axis=2)
    owners = pool_rows // local_pool_rows
    local_slot = pool_rows % local_pool_rows
    owned_here = owners == my_group
    slot_index = jnp.cumsum(owned_here.astype(jnp.int32), axis=1) - 1
    capacity_range = jnp.arange(capacity, dtype=jnp.int32)
    local_range = jnp.arange(local_pool_rows, dtype=jnp.int32)
    chosen = (
        owned_here[:, :, None, None]
        & (slot_index[:, :, None, None] == capacity_range[None, None, :, None])
        & (local_slot[:, :, None, None] == local_range[None, None, None, :])
    )
    selection = (
        jnp.sum(chosen.astype(jnp.float32), axis=1)
        .astype(jnp.bfloat16)
        .reshape(group_count * capacity, local_pool_rows)
    )

    def selected_rows(pool_table):
        flattened = pool_table.reshape(local_pool_rows, -1)
        picked = jnp.dot(selection, flattened, preferred_element_type=jnp.float32).astype(
            jnp.bfloat16
        )
        return picked.reshape((group_count * capacity,) + pool_table.shape[1:])

    group_token_rows = lax.dynamic_index_in_dim(pool_rows, my_group, 0, keepdims=False)
    group_owner = group_token_rows // local_pool_rows
    request_range = jnp.arange(requests, dtype=jnp.int32)
    earlier = request_range[None, :] < request_range[:, None]
    same_owner = group_owner[None, :] == group_owner[:, None]
    order_in_owner = jnp.sum((earlier & same_owner).astype(jnp.int32), axis=1)
    arrival = group_owner * capacity + order_in_owner
    down_panels = selected_rows(adapter_down_weight)
    received_down = lax.all_to_all(
        down_panels[:, :, : 3 * rank_width], "dp", split_axis=0, concat_axis=0, tiled=True
    )
    received_q = lax.all_to_all(
        selected_rows(adapter_up_query), "dp", split_axis=0, concat_axis=0, tiled=True
    )
    received_kv = lax.all_to_all(
        selected_rows(adapter_up_key_value), "dp", split_axis=0, concat_axis=0, tiled=True
    )
    fetched_down = jnp.take(received_down, arrival, axis=0)
    fetched_q = jnp.take(received_q, arrival, axis=0)
    fetched_kv = jnp.take(received_kv, arrival, axis=0)
    tokens_here = hidden.shape[1]
    token_total = tokens_here * seq_count
    longest = token_total // 4
    request_starts, owning_request, positions = layout(lengths[0], token_total)
    widths = (
        hidden.shape[2] // seq_count,
        base_query_weight.shape[2] // seq_count,
        base_key_weight.shape[2] // seq_count,
        base_value_weight.shape[2] // seq_count,
    )
    outgoing = jnp.concatenate(
        [
            part[0].reshape(tokens_here, seq_count, width)
            for part, width in zip(
                (hidden, base_query_weight, base_key_weight, base_value_weight), widths
            )
        ],
        axis=2,
    )
    arrived = [lax.dynamic_index_in_dim(outgoing, my_seat, 1, keepdims=False)]
    for shift in range(1, seq_count):
        target = (my_seat + shift) % seq_count
        piece = lax.dynamic_index_in_dim(outgoing, target, 1, keepdims=False)
        arrived.append(
            lax.ppermute(
                piece, "seq", [(i, (i + shift) % seq_count) for i in range(seq_count)]
            )
        )
    arrived = jnp.stack(arrived, axis=0)
    source_order = (my_seat - jnp.arange(seq_count, dtype=jnp.int32)) % seq_count
    gathered = jnp.take(arrived, source_order, axis=0).reshape(token_total, -1)
    edges = [0]
    for width in widths:
        edges.append(edges[-1] + width)
    features, query_head_rows, key_head_rows, value_head_rows = (
        gathered[:, edges[i] : edges[i + 1]] for i in range(4)
    )
    request_hot = (owning_request[:, None] == request_range[None, :])
    hot_f32 = request_hot.astype(jnp.float32)
    hot_bf16 = request_hot.astype(jnp.bfloat16)

    def down_select(inputs, panels):
        product = jnp.einsum("tf,rfc->trc", inputs, panels, preferred_element_type=jnp.float32)
        return jnp.sum(product * hot_f32[:, :, None], axis=1)

    def up_spread(rank_rows, panels):
        spread = (hot_bf16[:, :, None] * rank_rows[:, None, :]).reshape(token_total, -1)
        return jnp.dot(
            spread, panels.reshape(-1, panels.shape[-1]), preferred_element_type=jnp.float32
        )

    rank_terms = down_select(features, fetched_down)
    rank_terms, up_o_panels = lax.optimization_barrier(
        (rank_terms, selected_rows(adapter_up_output))
    )
    received_o = lax.all_to_all(up_o_panels, "dp", split_axis=0, concat_axis=0, tiled=True)
    fetched_o = jnp.take(received_o, arrival, axis=0)
    rank_shard = lax.psum_scatter(rank_terms, "seq", scatter_dimension=0, tiled=True)
    rank_shard, fetched_q, fetched_kv = lax.optimization_barrier((rank_shard, fetched_q, fetched_kv))
    ranks = lax.all_gather(rank_shard.astype(jnp.bfloat16), "seq", axis=0, tiled=True)

    query_delta = up_spread(ranks[:, :rank_width], fetched_q)
    key_delta = up_spread(ranks[:, rank_width : 2 * rank_width], fetched_kv[:, 0])
    value_delta = up_spread(ranks[:, 2 * rank_width :], fetched_kv[:, 1])
    query_local = query_head_rows.shape[1] // HEAD_SIZE
    local_key_value = key_head_rows.shape[1] // HEAD_SIZE
    group_length = query_local // local_key_value
    cosine_values, sine_values = rope_tables(positions, HEAD_SIZE)
    query_rows = rotate_halves(
        (query_head_rows.astype(jnp.float32) + adapter_scale * query_delta).reshape(
            token_total, query_local, HEAD_SIZE
        ),
        cosine_values,
        sine_values,
    ).astype(jnp.bfloat16)
    rotated_keys = rotate_halves(
        (key_head_rows.astype(jnp.float32) + adapter_scale * key_delta).reshape(
            token_total, local_key_value, HEAD_SIZE
        ),
        cosine_values,
        sine_values,
    ).astype(jnp.bfloat16)
    input_values = (
        (value_head_rows.astype(jnp.float32) + adapter_scale * value_delta)
        .astype(jnp.bfloat16)
        .reshape(token_total, local_key_value, HEAD_SIZE)
    )
    query_rows, down_o_panels = lax.optimization_barrier(
        (query_rows, down_panels[:, :, 3 * rank_width :])
    )
    received_down_o = lax.all_to_all(down_o_panels, "dp", split_axis=0, concat_axis=0, tiled=True)
    fetched_down_o = jnp.take(received_down_o, arrival, axis=0)
    context, up_full = attend_banded(
        query_rows.reshape(token_total, local_key_value, group_length, HEAD_SIZE),
        rotated_keys,
        input_values,
        owning_request,
        longest,
        lambda: lax.all_gather(fetched_o, "seq", axis=2, tiled=True),
    )
    rank_terms_o = down_select(context, fetched_down_o)
    context_rows = lax.all_to_all(context, "seq", split_axis=0, concat_axis=1, tiled=True)
    output_ranks = lax.psum_scatter(
        rank_terms_o.astype(jnp.bfloat16), "seq", scatter_dimension=0, tiled=True
    )
    my_requests = lax.dynamic_slice_in_dim(owning_request, my_seat * tokens_here, tokens_here, 0)
    onehot = (my_requests[:, None] == request_range[None, :]).astype(jnp.bfloat16)
    spread = (onehot[:, :, None] * output_ranks[:, None, :]).reshape(
        tokens_here, requests * rank_width
    )
    adapter_rows = (
        adapter_scale
        * jnp.dot(
            spread, up_full.reshape(requests * rank_width, -1), preferred_element_type=jnp.float32
        )
    ).astype(jnp.bfloat16)
    return (context_rows[None], adapter_rows[None])


def solution(mesh):
    placed = (
        P("dp", "seq", None),
        P("dp", "seq", None),
        P("dp", "seq", None),
        P("dp", "seq", None),
        P("dp", None),
        P(),
        P(),
        P("dp", "seq", None),
        P("dp", None, "seq"),
        P("dp", None, None, "seq"),
        P("dp", None, "seq"),
    )
    return jax.shard_map(
        body,
        mesh=mesh,
        in_specs=placed,
        out_specs=(P("dp", "seq", None), P("dp", "seq", None)),
        check_vma=False,
    )
```

```python
import math

import jax
import jax.numpy as jnp
from jax import lax
from jax.sharding import PartitionSpec as P

HEAD_SIZE = 128


adapter_scale = 2.0
rope_base = 500000.0


def layout(lengths_row, token_total):
    end_points = jnp.cumsum(lengths_row)
    request_starts = end_points - lengths_row
    positions = jnp.arange(token_total, dtype=jnp.int32)
    owning_request = jnp.sum((positions[:, None] >= end_points[None, :]).astype(jnp.int32), axis=1)
    matches = owning_request[:, None] == jnp.arange(lengths_row.shape[0], dtype=jnp.int32)[None, :]
    offsets = jnp.sum(jnp.where(matches, request_starts[None, :], 0), axis=1)
    return (request_starts, owning_request, positions - offsets)


def rope_tables(positions, head_dim):
    half_dim = head_dim // 2
    frequency = jnp.power(rope_base, -jnp.arange(half_dim, dtype=jnp.float32) * (2.0 / head_dim))
    angles = positions.astype(jnp.float32)[:, None] * frequency[None, :]
    return (jnp.cos(angles), jnp.sin(angles))


def rotate_halves(values, cosine_values, sine_values):
    half_dim = values.shape[-1] // 2
    first_half = values[..., :half_dim]
    second_half = values[..., half_dim:]
    cosines = cosine_values[:, None, :]
    sine_rows = sine_values[:, None, :]
    return jnp.concatenate(
        [
            first_half * cosines - second_half * sine_rows,
            second_half * cosines + first_half * sine_rows,
        ],
        axis=-1,
    )


def segment_mask(inputs, weights, request_starts, owning_request, longest):
    token_total = inputs.shape[0]

    def add_request(running, element):
        weight, start_row, request_index = element
        first_row = jnp.clip(start_row, 0, token_total - longest)
        block_rows = lax.dynamic_slice_in_dim(inputs, first_row, longest, 0)
        product = jnp.dot(block_rows, weight, preferred_element_type=jnp.float32)
        inside = lax.dynamic_slice_in_dim(owning_request, first_row, longest, 0) == request_index
        current = lax.dynamic_slice_in_dim(running, first_row, longest, 0)
        running = lax.dynamic_update_slice_in_dim(
            running, current + jnp.where(inside[:, None], product, 0.0), first_row, 0
        )
        return (running, None)

    initial = jnp.zeros((token_total, weights.shape[2]), jnp.float32)
    indices = jnp.arange(weights.shape[0], dtype=jnp.int32)
    result, unused = lax.scan(add_request, initial, (weights, request_starts, indices))
    return result


def attend_group(query_rows, key_head_rows, value_head_rows, owning_request):
    token_total = query_rows.shape[0]
    block_size = min(512, token_total)
    positions = jnp.arange(token_total, dtype=jnp.int32)

    def one_block(block_index):
        first_row = block_index * block_size
        query_block = lax.dynamic_slice_in_dim(query_rows, first_row, block_size, 0)
        own_request = lax.dynamic_slice_in_dim(owning_request, first_row, block_size, 0)
        own_position = first_row + jnp.arange(block_size, dtype=jnp.int32)
        allowed = (own_request[:, None] == owning_request[None, :]) & (
            positions[None, :] <= own_position[:, None]
        )
        scores = jnp.einsum(
            "qhgd,khd->hgqk", query_block, key_head_rows, preferred_element_type=jnp.float32
        ) / math.sqrt(HEAD_SIZE)
        scores = jnp.where(allowed[None, None], scores, -jnp.inf)
        row_top = jnp.max(scores, axis=-1, keepdims=True)
        weights = jnp.exp(scores - row_top)
        probabilities = (weights / jnp.sum(weights, axis=-1, keepdims=True)).astype(jnp.bfloat16)
        mixed = jnp.einsum(
            "hgqk,khd->qhgd", probabilities, value_head_rows, preferred_element_type=jnp.float32
        )
        return mixed.astype(jnp.bfloat16)

    blocks = lax.map(one_block, jnp.arange(token_total // block_size, dtype=jnp.int32))
    return blocks.reshape(token_total, -1)


def attend_banded(query_rows, key_head_rows, value_head_rows, owning_request, longest):
    token_total = query_rows.shape[0]
    block_size = min(256, token_total)
    blocks = []
    for block_index in range(token_total // block_size):
        first_row = block_index * block_size
        first_key = max(0, first_row - longest)
        last_key = first_row + block_size
        query_block = query_rows[first_row:last_key]
        key_block = key_head_rows[first_key:last_key]
        value_block = value_head_rows[first_key:last_key]
        own_request = owning_request[first_row:last_key]
        key_request = owning_request[first_key:last_key]
        own_position = first_row + jnp.arange(block_size, dtype=jnp.int32)
        key_position = first_key + jnp.arange(last_key - first_key, dtype=jnp.int32)
        allowed = (own_request[:, None] == key_request[None, :]) & (
            key_position[None, :] <= own_position[:, None]
        )
        scores = jnp.einsum(
            "qhgd,khd->hgqk", query_block, key_block, preferred_element_type=jnp.float32
        ) / math.sqrt(HEAD_SIZE)
        scores = jnp.where(allowed[None, None], scores, -jnp.inf)
        row_top = jnp.max(scores, axis=-1, keepdims=True)
        weights = jnp.exp(scores - row_top)
        probabilities = (weights / jnp.sum(weights, axis=-1, keepdims=True)).astype(jnp.bfloat16)
        mixed = jnp.einsum(
            "hgqk,khd->qhgd", probabilities, value_block, preferred_element_type=jnp.float32
        )
        blocks.append(mixed.astype(jnp.bfloat16).reshape(block_size, -1))
    return jnp.concatenate(blocks, axis=0)


def body(
    hidden,
    base_query_weight,
    base_key_weight,
    base_value_weight,
    lengths,
    request_adapter,
    adapter_pool_row,
    adapter_down_weight,
    adapter_up_query,
    adapter_up_key_value,
    adapter_up_output,
):
    group_count = lax.axis_size("dp")
    seq_count = lax.axis_size("seq")
    my_group = lax.axis_index("dp")
    my_seat = lax.axis_index("seq")
    local_pool_rows = adapter_down_weight.shape[0]
    requests = request_adapter.shape[1]
    capacity = (2 * requests + group_count - 1) // group_count
    rank_width = adapter_up_query.shape[1]
    adapter_count = adapter_pool_row.shape[0]
    matches = (
        request_adapter[:, :, None] == jnp.arange(adapter_count, dtype=jnp.int32)[None, None, :]
    )
    pool_rows = jnp.sum(jnp.where(matches, adapter_pool_row[None, None, :], 0), axis=2)
    owners = pool_rows // local_pool_rows
    local_slot = pool_rows % local_pool_rows
    owned_here = owners == my_group
    slot_index = jnp.cumsum(owned_here.astype(jnp.int32), axis=1) - 1
    capacity_range = jnp.arange(capacity, dtype=jnp.int32)
    local_range = jnp.arange(local_pool_rows, dtype=jnp.int32)
    chosen = (
        owned_here[:, :, None, None]
        & (slot_index[:, :, None, None] == capacity_range[None, None, :, None])
        & (local_slot[:, :, None, None] == local_range[None, None, None, :])
    )
    selection = (
        jnp.sum(chosen.astype(jnp.float32), axis=1)
        .astype(jnp.bfloat16)
        .reshape(group_count * capacity, local_pool_rows)
    )

    def selected_rows(pool_table):
        flattened = pool_table.reshape(local_pool_rows, -1)
        picked = jnp.dot(selection, flattened, preferred_element_type=jnp.float32).astype(
            jnp.bfloat16
        )
        return picked.reshape((group_count * capacity,) + pool_table.shape[1:])

    group_token_rows = lax.dynamic_index_in_dim(pool_rows, my_group, 0, keepdims=False)
    group_owner = group_token_rows // local_pool_rows
    request_range = jnp.arange(requests, dtype=jnp.int32)
    earlier = request_range[None, :] < request_range[:, None]
    same_owner = group_owner[None, :] == group_owner[:, None]
    order_in_owner = jnp.sum((earlier & same_owner).astype(jnp.int32), axis=1)
    arrival = group_owner * capacity + order_in_owner
    received_o = lax.all_to_all(
        selected_rows(adapter_up_output), "dp", split_axis=0, concat_axis=0, tiled=True
    )
    down_panels = selected_rows(adapter_down_weight)
    received_down = lax.all_to_all(
        down_panels[:, :, : 3 * rank_width], "dp", split_axis=0, concat_axis=0, tiled=True
    )
    query_size = adapter_up_query[0].size
    up_rows = jnp.concatenate(
        [
            adapter_up_query.reshape(local_pool_rows, -1),
            adapter_up_key_value.reshape(local_pool_rows, -1),
        ],
        axis=1,
    )
    received_up = lax.all_to_all(selected_rows(up_rows), "dp", split_axis=0, concat_axis=0, tiled=True)
    received_q = received_up[:, :query_size].reshape((-1,) + adapter_up_query.shape[1:])
    received_kv = received_up[:, query_size:].reshape((-1,) + adapter_up_key_value.shape[1:])
    fetched_o = jnp.take(received_o, arrival, axis=0)
    fetched_down = jnp.take(received_down, arrival, axis=0)
    fetched_q = jnp.take(received_q, arrival, axis=0)
    fetched_kv = jnp.take(received_kv, arrival, axis=0)
    tokens_here = hidden.shape[1]
    token_total = tokens_here * seq_count
    longest = token_total // 4
    request_starts, owning_request, positions = layout(lengths[0], token_total)
    widths = (
        hidden.shape[2] // seq_count,
        base_query_weight.shape[2] // seq_count,
        base_key_weight.shape[2] // seq_count,
        base_value_weight.shape[2] // seq_count,
    )
    outgoing = jnp.concatenate(
        [
            part[0].reshape(tokens_here, seq_count, width)
            for part, width in zip(
                (hidden, base_query_weight, base_key_weight, base_value_weight), widths
            )
        ],
        axis=2,
    )
    arrived = [lax.dynamic_index_in_dim(outgoing, my_seat, 1, keepdims=False)]
    for shift in range(1, seq_count):
        target = (my_seat + shift) % seq_count
        piece = lax.dynamic_index_in_dim(outgoing, target, 1, keepdims=False)
        arrived.append(
            lax.ppermute(
                piece, "seq", [(i, (i + shift) % seq_count) for i in range(seq_count)]
            )
        )
    arrived = jnp.stack(arrived, axis=0)
    source_order = (my_seat - jnp.arange(seq_count, dtype=jnp.int32)) % seq_count
    gathered = jnp.take(arrived, source_order, axis=0).reshape(token_total, -1)
    edges = [0]
    for width in widths:
        edges.append(edges[-1] + width)
    features, query_head_rows, key_head_rows, value_head_rows = (
        gathered[:, edges[i] : edges[i + 1]] for i in range(4)
    )
    up_full = lax.all_gather(fetched_o, "seq", axis=2, tiled=True)
    up_full, features = lax.optimization_barrier((up_full, features))
    request_hot = (owning_request[:, None] == request_range[None, :])
    hot_f32 = request_hot.astype(jnp.float32)
    hot_bf16 = request_hot.astype(jnp.bfloat16)

    def down_select(inputs, panels):
        product = jnp.einsum("tf,rfc->trc", inputs, panels, preferred_element_type=jnp.float32)
        return jnp.sum(product * hot_f32[:, :, None], axis=1)

    def up_spread(rank_rows, panels):
        spread = (hot_bf16[:, :, None] * rank_rows[:, None, :]).reshape(token_total, -1)
        return jnp.dot(
            spread, panels.reshape(-1, panels.shape[-1]), preferred_element_type=jnp.float32
        )

    rank_terms = down_select(features, fetched_down)
    rank_shard = lax.psum_scatter(rank_terms, "seq", scatter_dimension=0, tiled=True)
    rank_shard, down_o_panels = lax.optimization_barrier(
        (rank_shard, down_panels[:, :, 3 * rank_width :])
    )
    ranks = lax.all_gather(rank_shard.astype(jnp.bfloat16), "seq", axis=0, tiled=True)
    received_down_o = lax.all_to_all(down_o_panels, "dp", split_axis=0, concat_axis=0, tiled=True)
    fetched_down_o = jnp.take(received_down_o, arrival, axis=0)
    query_delta = up_spread(ranks[:, :rank_width], fetched_q)
    key_delta = up_spread(ranks[:, rank_width : 2 * rank_width], fetched_kv[:, 0])
    value_delta = up_spread(ranks[:, 2 * rank_width :], fetched_kv[:, 1])
    query_local = query_head_rows.shape[1] // HEAD_SIZE
    local_key_value = key_head_rows.shape[1] // HEAD_SIZE
    group_length = query_local // local_key_value
    cosine_values, sine_values = rope_tables(positions, HEAD_SIZE)
    query_rows = rotate_halves(
        (query_head_rows.astype(jnp.float32) + adapter_scale * query_delta).reshape(
            token_total, query_local, HEAD_SIZE
        ),
        cosine_values,
        sine_values,
    ).astype(jnp.bfloat16)
    rotated_keys = rotate_halves(
        (key_head_rows.astype(jnp.float32) + adapter_scale * key_delta).reshape(
            token_total, local_key_value, HEAD_SIZE
        ),
        cosine_values,
        sine_values,
    ).astype(jnp.bfloat16)
    input_values = (
        (value_head_rows.astype(jnp.float32) + adapter_scale * value_delta)
        .astype(jnp.bfloat16)
        .reshape(token_total, local_key_value, HEAD_SIZE)
    )
    context = attend_banded(
        query_rows.reshape(token_total, local_key_value, group_length, HEAD_SIZE),
        rotated_keys,
        input_values,
        owning_request,
        longest,
    )
    rank_terms_o = down_select(context, fetched_down_o)
    context_rows = lax.all_to_all(context, "seq", split_axis=0, concat_axis=1, tiled=True)
    output_ranks = lax.psum_scatter(
        rank_terms_o.astype(jnp.bfloat16), "seq", scatter_dimension=0, tiled=True
    )
    my_requests = lax.dynamic_slice_in_dim(owning_request, my_seat * tokens_here, tokens_here, 0)
    onehot = (my_requests[:, None] == request_range[None, :]).astype(jnp.bfloat16)
    spread = (onehot[:, :, None] * output_ranks[:, None, :]).reshape(
        tokens_here, requests * rank_width
    )
    adapter_rows = (
        adapter_scale
        * jnp.dot(
            spread, up_full.reshape(requests * rank_width, -1), preferred_element_type=jnp.float32
        )
    ).astype(jnp.bfloat16)
    return (context_rows[None], adapter_rows[None])


def solution(mesh):
    placed = (
        P("dp", "seq", None),
        P("dp", "seq", None),
        P("dp", "seq", None),
        P("dp", "seq", None),
        P("dp", None),
        P(),
        P(),
        P("dp", "seq", None),
        P("dp", None, "seq"),
        P("dp", None, None, "seq"),
        P("dp", None, "seq"),
    )
    return jax.shard_map(
        body,
        mesh=mesh,
        in_specs=placed,
        out_specs=(P("dp", "seq", None), P("dp", "seq", None)),
        check_vma=False,
    )
```
